256 devices in a mesh: row: 16 (over z, y_hi), col: 16 (over x, y_lo, core).
Axes of the slice: x: 4, y: 4 (y_hi: 2, y_lo: 2; y = y_hi * 2 + y_lo), z: 8, core: 2. Of those that a mesh axis runs over, the one named last changes fastest.
Arguments:
- queries: bfloat16 [32, 2048, 128], P('row', 'col'), may hold values from -6.5 to 6.5
- keys: bfloat16 [32, 2048, 128], P('row', 'col'), may hold values from -6.5 to 6.5
- values: bfloat16 [32, 2048, 128], P('row', 'col'), may hold values from -6 to 6
- gate: bfloat16 [32, 2048, 128], P('row', 'col'), may hold values from -6 to 6
- bias: bfloat16 [4, 2048, 2048], P(None, 'col'), may hold values from -7.5 to 7.5
- grad_out: bfloat16 [32, 2048, 128], P('row', 'col'), may hold values from -6 to 6
- block_mask: int32 [16, 16], replicated, may hold values from 0 to 1, as said below
Outputs:
- query_grad: bfloat16 [32, 2048, 128], P('row', 'col')
- key_grad: bfloat16 [32, 2048, 128], P('row', 'col')
- value_grad: bfloat16 [32, 2048, 128], P('row', 'col')
- gate_grad: bfloat16 [32, 2048, 128], P('row', 'col')
- bias_grad: float32 [4, 2048, 2048], P(None, 'col', 'row')
The draws below stay inside these ranges and needn't reach their ends.
Inputs may be any that keep to these rules, and one draw needn't show every extreme that they name: `block_mask`: every diagonal block is 1.
All inputs are finite; a program needn't handle non-finite values.
Results may differ from the reference program's by a relative error of at most 0.02.
Values may be sent and summed in bfloat16 or wider, within the bound.
No kernel may reach another device: no remote copies, remote signals or barrier semaphores. Data moves between devices by JAX's collectives and lax.ppermute only.
A program may use at most 64 MiB of HBM per device.

```python
import math
import jax
import jax.numpy as jnp
from jax import lax

H = 4
DH = 32
BLK = 128
L = 2048
R = 32
NB = 16


def drawn_pair(key):
    shape = (R, L, H * DH)
    query_out = jnp.clip(jax.random.normal(jax.random.fold_in(key, 11), shape, jnp.float32), -4.0, 4.0)
    key_out = jnp.clip(jax.random.normal(jax.random.fold_in(key, 12), shape, jnp.float32), -4.0, 4.0)
    return (query_out, key_out)


def draw_queries(key, part):
    return drawn_pair(key)[0].astype(jnp.bfloat16)


def draw_keys(key, part):
    return drawn_pair(key)[1].astype(jnp.bfloat16)


def draw_block_mask(key, part):
    level = jax.random.permutation(jax.random.fold_in(key, 21), NB) % 8
    roll = jax.random.randint(jax.random.fold_in(key, 22), (NB, NB), 0, 8)
    diagonal = jnp.arange(NB)[:, None] == jnp.arange(NB)[None, :]
    return jnp.where((roll <= level[:, None]) | diagonal, 1, 0).astype(jnp.int32)


def block_levels(own_key, dims, pieces, low, top_value):
    gain = 1.0
    for dim, blocks in pieces:
        steps = jax.random.uniform(jax.random.fold_in(jax.random.fold_in(own_key, 6), dim), (blocks,), jnp.float32, low / len(pieces), top_value / len(pieces))
        gain = gain * jnp.repeat(jnp.exp(steps), dims[dim] // blocks).reshape((-1,) + (1,) * (len(dims) - 1 - dim))
    return gain


def noise(key, dims, scale, bound, cuts=(), held_as=jnp.bfloat16):
    factor_of = block_levels(key, dims, cuts, -0.22, 0.18) if cuts else 1.0
    result = jax.random.normal(key, dims, jnp.float32) * scale * factor_of
    return jnp.minimum(jnp.maximum(result, -bound), bound).astype(held_as)


def setup_inputs(seed: int = 0) -> dict:
    splits = jax.random.split(jax.random.key(seed), 8)
    queries = draw_queries(jax.random.fold_in(splits[7], 71), 0)
    keys = draw_keys(jax.random.fold_in(splits[7], 71), 0)
    values = noise(splits[2], (R, L, H * DH), 1.0, 6.0, ((0, 16), (1, 16)))
    gate = noise(splits[3], (R, L, H * DH), 1.5, 6.0, ((0, 16), (1, 16)))
    bias = noise(splits[4], (H, L, L), 1.5, 7.5, ((1, 16),))
    grad_out = noise(splits[5], (R, L, H * DH), 1.0, 6.0, ((0, 16), (1, 16)))
    block_mask = draw_block_mask(jax.random.fold_in(splits[7], 71), 0)
    return dict(queries=queries, keys=keys, values=values, gate=gate, bias=bias, grad_out=grad_out, block_mask=block_mask)


NEGATIVE = -1000000000.0

def reference(queries, keys, values, gate, bias, grad_out, block_mask):
    score_scale = 1.0 / math.sqrt(DH)
    allowed = jnp.repeat(jnp.repeat(block_mask, BLK, axis=0), BLK, axis=1) > 0
    bias_full = bias.astype(jnp.float32)

    def one_row(running, slab_row):
        query_row, key_row, value_row, gate_row, cotangent_row = slab_row
        query_heads = query_row.astype(jnp.float32).reshape(L, H, DH)
        key_heads = key_row.astype(jnp.float32).reshape(L, H, DH)
        value_heads = value_row.astype(jnp.float32).reshape(L, H, DH)
        scores = jnp.einsum('jhd,khd->hjk', query_heads, key_heads) * score_scale + bias_full
        scores = jnp.where(allowed[None], scores, NEGATIVE)
        row_top = lax.optimization_barrier(jnp.max(scores, axis=2, keepdims=True))
        log_total = row_top + jnp.log(lax.optimization_barrier(jnp.sum(jnp.exp(scores - row_top), axis=2, keepdims=True)))
        weights = jnp.exp(scores - log_total)
        weights_b = lax.optimization_barrier(weights.astype(jnp.bfloat16)).astype(jnp.float32)
        attended = jnp.einsum('hjk,khd->jhd', weights_b, value_heads)
        gate_sig = jax.nn.sigmoid(gate_row.astype(jnp.float32)).reshape(L, H, DH)
        cotangent = cotangent_row.astype(jnp.float32).reshape(L, H, DH)
        gate_grad = (cotangent * attended * gate_sig * (1.0 - gate_sig)).astype(jnp.bfloat16)
        out_grad = lax.optimization_barrier((cotangent * gate_sig).astype(jnp.bfloat16)).astype(jnp.float32)
        grad_dot = jnp.transpose(lax.optimization_barrier(jnp.sum(out_grad * attended, axis=2)))
        prob_grad = jnp.einsum('jhd,khd->hjk', out_grad, value_heads)
        score_grad = weights * (prob_grad - grad_dot[:, :, None])
        score_grad_b = lax.optimization_barrier(score_grad.astype(jnp.bfloat16)).astype(jnp.float32)
        query_grad = jnp.einsum('hjk,khd->jhd', score_grad_b, key_heads) * score_scale
        key_grad = jnp.einsum('hjk,jhd->khd', score_grad_b, query_heads) * score_scale
        value_grad = jnp.einsum('hjk,jhd->khd', weights_b, out_grad)
        results = (query_grad.astype(jnp.bfloat16).reshape(L, H * DH), key_grad.astype(jnp.bfloat16).reshape(L, H * DH), value_grad.astype(jnp.bfloat16).reshape(L, H * DH), gate_grad.reshape(L, H * DH))
        return (running + score_grad, results)
    initial = jnp.zeros((H, L, L), jnp.float32)
    bias_grad, stacked = lax.scan(one_row, initial, (queries, keys, values, gate, grad_out))
    return (stacked[0], stacked[1], stacked[2], stacked[3], bias_grad)
```

```python
import math

import jax
import jax.numpy as jnp
from jax import lax
from jax.sharding import PartitionSpec as P

H = 4
DH = 32
BLK = 128


NEGATIVE = -1000000000.0


def block_flags(block_mask, first_row, row_count, key_block):
    block_ids = (first_row + jnp.arange(row_count, dtype=jnp.int32)) // BLK
    column = lax.dynamic_index_in_dim(block_mask, key_block, axis=1, keepdims=False)
    matching = block_ids[:, None] == jnp.arange(block_mask.shape[0], dtype=jnp.int32)[None, :]
    return jnp.sum(jnp.where(matching, column[None, :], 0), axis=1) > 0


def tile_scores(query_tile, key_tile, bias_tile, allowed, score_scale):
    products = jnp.einsum(
        "rjhd,rkhd->rhjk", query_tile, key_tile, preferred_element_type=jnp.float32
    )
    scores = products * score_scale + bias_tile.astype(jnp.float32)[None]
    return jnp.where(allowed[None, None, :, None], scores, NEGATIVE)


def tile_grads(
    query_tile, key_tile, value_tile, bias_tile, allowed, log_total, grad_dot, out_grad, score_scale
):
    scores = tile_scores(query_tile, key_tile, bias_tile, allowed, score_scale)
    weights = jnp.exp(scores - log_total[..., None])
    prob_grad = jnp.einsum(
        "rjhd,rkhd->rhjk", out_grad, value_tile, preferred_element_type=jnp.float32
    )
    return (weights, weights * (prob_grad - grad_dot[..., None]))


def local(queries, keys, values, gate, bias, grad_out, block_mask):
    slab_rows, local_cols, channels = queries.shape
    head_count = H
    head_size = DH
    score_scale = 1.0 / math.sqrt(head_size)
    col_start = lax.axis_index("col") * local_cols
    key_all, value_all = (
        lax.all_gather(keys, "col", axis=1, tiled=True),
        lax.all_gather(values, "col", axis=1, tiled=True),
    )
    all_cols = key_all.shape[1]
    blocks = all_cols // BLK
    query_heads = queries.reshape(slab_rows, local_cols, head_count, head_size)
    key_heads_all = key_all.reshape(slab_rows, all_cols, head_count, head_size)
    value_heads_all = value_all.reshape(slab_rows, all_cols, head_count, head_size)

    def key_slices(key_block):
        offset = key_block * BLK
        return (
            lax.dynamic_slice_in_dim(key_heads_all, offset, BLK, 1),
            lax.dynamic_slice_in_dim(value_heads_all, offset, BLK, 1),
            lax.dynamic_slice_in_dim(bias, offset, BLK, 2),
            block_flags(block_mask, col_start, local_cols, key_block),
        )

    def stats_step(key_block, carried):
        key_tile, value_tile, bias_tile, allowed = key_slices(key_block)

        def stats_update(state_in):
            row_top, row_mass = state_in
            scores = tile_scores(query_heads, key_tile, bias_tile, allowed, score_scale)
            new_top = jnp.maximum(row_top, jnp.max(scores, axis=3))
            row_mass = row_mass * jnp.exp(row_top - new_top) + jnp.sum(
                jnp.exp(scores - new_top[..., None]), axis=3
            )
            return (new_top, row_mass)

        return lax.cond(jnp.any(allowed), stats_update, lambda kept: kept, carried)

    stat_shape = (slab_rows, head_count, local_cols)
    row_top, row_mass = lax.fori_loop(
        0,
        blocks,
        stats_step,
        (jnp.full(stat_shape, -1e30, jnp.float32), jnp.zeros(stat_shape, jnp.float32)),
    )
    log_total = row_top + jnp.log(row_mass)

    def attend_step(key_block, carried):
        key_tile, value_tile, bias_tile, allowed = key_slices(key_block)

        def attend_update(running):
            scores = tile_scores(query_heads, key_tile, bias_tile, allowed, score_scale)
            probs = jnp.exp(scores - log_total[..., None]).astype(jnp.bfloat16)
            return running + jnp.einsum(
                "rhjk,rkhd->rjhd", probs, value_tile, preferred_element_type=jnp.float32
            )

        return lax.cond(jnp.any(allowed), attend_update, lambda kept: kept, carried)

    attended = lax.fori_loop(
        0,
        blocks,
        attend_step,
        jnp.zeros((slab_rows, local_cols, head_count, head_size), jnp.float32),
    )
    gate_sig = jax.nn.sigmoid(gate.astype(jnp.float32)).reshape(
        slab_rows, local_cols, head_count, head_size
    )
    cotangent = grad_out.astype(jnp.float32).reshape(slab_rows, local_cols, head_count, head_size)
    gate_grad = (
        (cotangent * attended * gate_sig * (1.0 - gate_sig))
        .astype(jnp.bfloat16)
        .reshape(slab_rows, local_cols, channels)
    )
    out_grad = (cotangent * gate_sig).astype(jnp.bfloat16)
    grad_dot = jnp.transpose(jnp.sum(out_grad.astype(jnp.float32) * attended, axis=3), (0, 2, 1))

    def grad_step(key_block, carried):
        key_tile, value_tile, bias_tile, allowed = key_slices(key_block)

        def grad_update(state_in):
            query_acc, bias_part, kv_part = state_in
            weights, score_grad = tile_grads(
                query_heads,
                key_tile,
                value_tile,
                bias_tile,
                allowed,
                log_total,
                grad_dot,
                out_grad,
                score_scale,
            )
            score_grad_b = score_grad.astype(jnp.bfloat16)
            query_acc = query_acc + jnp.einsum(
                "rhjk,rkhd->rjhd", score_grad_b, key_tile, preferred_element_type=jnp.float32
            )
            offset = key_block * BLK
            bias_part = lax.dynamic_update_slice_in_dim(
                bias_part, jnp.sum(score_grad, axis=0).astype(jnp.bfloat16), offset, 2
            )
            key_piece = jnp.einsum(
                "rhjk,rjhd->rkhd", score_grad_b, query_heads, preferred_element_type=jnp.float32
            )
            value_piece = jnp.einsum(
                "rhjk,rjhd->rkhd",
                weights.astype(jnp.bfloat16),
                out_grad,
                preferred_element_type=jnp.float32,
            )
            piece = jnp.concatenate(
                (
                    key_piece.reshape(slab_rows, BLK, channels),
                    value_piece.reshape(slab_rows, BLK, channels),
                ),
                axis=2,
            ).astype(jnp.bfloat16)
            kv_part = lax.dynamic_update_slice_in_dim(kv_part, piece, offset, 1)
            return (query_acc, bias_part, kv_part)

        return lax.cond(jnp.any(allowed), grad_update, lambda kept: kept, carried)

    initial = (
        jnp.zeros((slab_rows, local_cols, head_count, head_size), jnp.float32),
        jnp.zeros((head_count, local_cols, all_cols), jnp.bfloat16),
        jnp.zeros((slab_rows, all_cols, 2 * channels), jnp.bfloat16),
    )
    query_acc, bias_part, kv_part = lax.fori_loop(0, blocks, grad_step, initial)
    col_count = all_cols // local_cols
    kv_moved = lax.all_to_all(
        kv_part.reshape(slab_rows, col_count, local_cols, 2 * channels), "col", 1, 1, tiled=True
    )
    kv_sum = jnp.sum(kv_moved.astype(jnp.float32), axis=1)
    key_grad = (kv_sum[..., :channels] * score_scale).astype(jnp.bfloat16)
    value_grad = kv_sum[..., channels:].astype(jnp.bfloat16)
    row_count = lax.axis_size("row")
    row_keys = all_cols // row_count
    bias_moved = lax.all_to_all(
        bias_part.reshape(head_count, local_cols, row_count, row_keys), "row", 2, 2, tiled=True
    )
    bias_grad = jnp.sum(bias_moved.astype(jnp.float32), axis=2)
    query_grad = (
        (query_acc * score_scale).astype(jnp.bfloat16).reshape(slab_rows, local_cols, channels)
    )
    return (query_grad, key_grad, value_grad, gate_grad, bias_grad)


def solution(mesh):
    return jax.shard_map(
        local,
        mesh=mesh,
        in_specs=(
            P("row", "col", None),
            P("row", "col", None),
            P("row", "col", None),
            P("row", "col", None),
            P(None, "col", None),
            P("row", "col", None),
            P(),
        ),
        out_specs=(
            P("row", "col", None),
            P("row", "col", None),
            P("row", "col", None),
            P("row", "col", None),
            P(None, "col", "row"),
        ),
        check_vma=False,
    )
```

```python
import math

import jax
import jax.numpy as jnp
from jax import lax
from jax.sharding import PartitionSpec as P

H = 4
DH = 32
BLK = 128
GROUPS = 2


NEGATIVE = -1000000000.0


def block_flags(block_mask, first_row, row_count):
    block_ids = (first_row + jnp.arange(row_count, dtype=jnp.int32)) // BLK
    rows = jnp.take(block_mask, block_ids, axis=0)
    return rows > 0


def tile_scores(query_tile, key_tile, bias_tile, allowed, score_scale):
    products = jnp.einsum(
        "rjhd,rkhd->rhjk", query_tile, key_tile, preferred_element_type=jnp.float32
    )
    scores = products * score_scale + bias_tile.astype(jnp.float32)[None]
    return jnp.where(allowed[None, None, :, None], scores, NEGATIVE)


def tile_grads(
    query_tile, key_tile, value_tile, bias_tile, allowed, log_total, grad_dot, out_grad, score_scale
):
    scores = tile_scores(query_tile, key_tile, bias_tile, allowed, score_scale)
    weights = jnp.exp(scores - log_total[..., None])
    prob_grad = jnp.einsum(
        "rjhd,rkhd->rhjk", out_grad, value_tile, preferred_element_type=jnp.float32
    )
    return (weights, weights * (prob_grad - grad_dot[..., None]))


def head_group(queries, keys, values, gate, bias, grad_out, flags, head_count):
    slab_rows, local_cols, channels = queries.shape
    head_size = DH
    score_scale = 1.0 / math.sqrt(head_size)
    key_all, value_all = (
        lax.all_gather(keys, "col", axis=1, tiled=True),
        lax.all_gather(values, "col", axis=1, tiled=True),
    )
    all_cols = key_all.shape[1]
    blocks = all_cols // BLK
    query_heads = queries.reshape(slab_rows, local_cols, head_count, head_size)
    key_heads_all = key_all.reshape(slab_rows, all_cols, head_count, head_size)
    value_heads_all = value_all.reshape(slab_rows, all_cols, head_count, head_size)

    def key_slices(key_block):
        offset = key_block * BLK
        return (
            lax.dynamic_slice_in_dim(key_heads_all, offset, BLK, 1),
            lax.dynamic_slice_in_dim(value_heads_all, offset, BLK, 1),
            lax.dynamic_slice_in_dim(bias, offset, BLK, 2),
            lax.dynamic_index_in_dim(flags, key_block, axis=1, keepdims=False),
        )

    def stats_step(key_block, carried):
        key_tile, value_tile, bias_tile, allowed = key_slices(key_block)

        def stats_update(state_in):
            row_top, row_mass = state_in
            scores = tile_scores(query_heads, key_tile, bias_tile, allowed, score_scale)
            new_top = jnp.maximum(row_top, jnp.max(scores, axis=3))
            row_mass = row_mass * jnp.exp(row_top - new_top) + jnp.sum(
                jnp.exp(scores - new_top[..., None]), axis=3
            )
            return (new_top, row_mass)

        return lax.cond(jnp.any(allowed), stats_update, lambda kept: kept, carried)

    stat_shape = (slab_rows, head_count, local_cols)
    row_top, row_mass = lax.fori_loop(
        0,
        blocks,
        stats_step,
        (jnp.full(stat_shape, -1e30, jnp.float32), jnp.zeros(stat_shape, jnp.float32)),
    )
    log_total = row_top + jnp.log(row_mass)

    def attend_step(key_block, carried):
        key_tile, value_tile, bias_tile, allowed = key_slices(key_block)

        def attend_update(running):
            scores = tile_scores(query_heads, key_tile, bias_tile, allowed, score_scale)
            probs = jnp.exp(scores - log_total[..., None]).astype(jnp.bfloat16)
            return running + jnp.einsum(
                "rhjk,rkhd->rjhd", probs, value_tile, preferred_element_type=jnp.float32
            )

        return lax.cond(jnp.any(allowed), attend_update, lambda kept: kept, carried)

    attended = lax.fori_loop(
        0,
        blocks,
        attend_step,
        jnp.zeros((slab_rows, local_cols, head_count, head_size), jnp.float32),
    )
    gate_sig = jax.nn.sigmoid(gate.astype(jnp.float32)).reshape(
        slab_rows, local_cols, head_count, head_size
    )
    cotangent = grad_out.astype(jnp.float32).reshape(slab_rows, local_cols, head_count, head_size)
    gate_grad = (
        (cotangent * attended * gate_sig * (1.0 - gate_sig))
        .astype(jnp.bfloat16)
        .reshape(slab_rows, local_cols, channels)
    )
    out_grad = (cotangent * gate_sig).astype(jnp.bfloat16)
    grad_dot = jnp.transpose(jnp.sum(out_grad.astype(jnp.float32) * attended, axis=3), (0, 2, 1))

    def grad_step(key_block, carried):
        key_tile, value_tile, bias_tile, allowed = key_slices(key_block)

        def grad_update(state_in):
            query_acc, bias_part, kv_part = state_in
            weights, score_grad = tile_grads(
                query_heads,
                key_tile,
                value_tile,
                bias_tile,
                allowed,
                log_total,
                grad_dot,
                out_grad,
                score_scale,
            )
            score_grad_b = score_grad.astype(jnp.bfloat16)
            query_acc = query_acc + jnp.einsum(
                "rhjk,rkhd->rjhd", score_grad_b, key_tile, preferred_element_type=jnp.float32
            )
            offset = key_block * BLK
            bias_part = lax.dynamic_update_slice_in_dim(
                bias_part, jnp.sum(score_grad, axis=0).astype(jnp.bfloat16), offset, 2
            )
            key_piece = jnp.einsum(
                "rhjk,rjhd->rkhd", score_grad_b, query_heads, preferred_element_type=jnp.float32
            )
            value_piece = jnp.einsum(
                "rhjk,rjhd->rkhd",
                weights.astype(jnp.bfloat16),
                out_grad,
                preferred_element_type=jnp.float32,
            )
            piece = jnp.concatenate(
                (
                    key_piece.reshape(slab_rows, BLK, channels),
                    value_piece.reshape(slab_rows, BLK, channels),
                ),
                axis=2,
            ).astype(jnp.bfloat16)
            kv_part = lax.dynamic_update_slice_in_dim(kv_part, piece, offset, 1)
            return (query_acc, bias_part, kv_part)

        return lax.cond(jnp.any(allowed), grad_update, lambda kept: kept, carried)

    initial = (
        jnp.zeros((slab_rows, local_cols, head_count, head_size), jnp.float32),
        jnp.zeros((head_count, local_cols, all_cols), jnp.bfloat16),
        jnp.zeros((slab_rows, all_cols, 2 * channels), jnp.bfloat16),
    )
    query_acc, bias_part, kv_part = lax.fori_loop(0, blocks, grad_step, initial)
    col_count = all_cols // local_cols
    kv_moved = lax.all_to_all(
        kv_part.reshape(slab_rows, col_count, local_cols, 2 * channels), "col", 1, 1, tiled=True
    )
    kv_sum = jnp.sum(kv_moved.astype(jnp.float32), axis=1)
    key_grad = (kv_sum[..., :channels] * score_scale).astype(jnp.bfloat16)
    value_grad = kv_sum[..., channels:].astype(jnp.bfloat16)
    row_count = lax.axis_size("row")
    row_keys = all_cols // row_count
    bias_moved = lax.all_to_all(
        bias_part.reshape(head_count, local_cols, row_count, row_keys), "row", 2, 2, tiled=True
    )
    bias_grad = jnp.sum(bias_moved.astype(jnp.float32), axis=2)
    query_grad = (
        (query_acc * score_scale).astype(jnp.bfloat16).reshape(slab_rows, local_cols, channels)
    )
    return (query_grad, key_grad, value_grad, gate_grad, bias_grad)


def local(queries, keys, values, gate, bias, grad_out, block_mask):
    local_cols = queries.shape[1]
    col_start = lax.axis_index("col") * local_cols
    flags = block_flags(block_mask, col_start, local_cols)
    heads_per = H // GROUPS
    width = heads_per * DH
    pieces = []
    for group in range(GROUPS):
        lo = group * width
        pieces.append(
            head_group(
                queries[..., lo : lo + width],
                keys[..., lo : lo + width],
                values[..., lo : lo + width],
                gate[..., lo : lo + width],
                bias[group * heads_per : (group + 1) * heads_per],
                grad_out[..., lo : lo + width],
                flags,
                heads_per,
            )
        )
    query_grad, key_grad, value_grad, gate_grad = (
        jnp.concatenate([piece[n] for piece in pieces], axis=2) for n in range(4)
    )
    bias_grad = jnp.concatenate([piece[4] for piece in pieces], axis=0)
    return (query_grad, key_grad, value_grad, gate_grad, bias_grad)


def solution(mesh):
    return jax.shard_map(
        local,
        mesh=mesh,
        in_specs=(
            P("row", "col", None),
            P("row", "col", None),
            P("row", "col", None),
            P("row", "col", None),
            P(None, "col", None),
            P("row", "col", None),
            P(),
        ),
        out_specs=(
            P("row", "col", None),
            P("row", "col", None),
            P("row", "col", None),
            P("row", "col", None),
            P(None, "col", "row"),
        ),
        check_vma=False,
    )
```

```python
import math

import jax
import jax.numpy as jnp
from jax import lax
from jax.sharding import PartitionSpec as P

H = 4
DH = 32
BLK = 128


NEGATIVE = -1000000000.0


def local(queries, keys, values, gate, bias, grad_out, block_mask):
    slab_rows, local_cols, channels = queries.shape
    head_count = H
    head_size = DH
    score_scale = 1.0 / math.sqrt(head_size)
    col_start = lax.axis_index("col") * local_cols
    key_all = lax.all_gather(keys, "col", axis=1, tiled=True)
    value_all = lax.all_gather(values, "col", axis=1, tiled=True)
    all_cols = key_all.shape[1]
    query_heads = queries.reshape(slab_rows, local_cols, head_count, head_size)
    key_heads = key_all.reshape(slab_rows, all_cols, head_count, head_size)
    value_heads = value_all.reshape(slab_rows, all_cols, head_count, head_size)

    block_ids = (col_start + jnp.arange(local_cols, dtype=jnp.int32)) // BLK
    allowed = jnp.repeat(jnp.take(block_mask, block_ids, axis=0), BLK, axis=1) > 0

    products = jnp.einsum(
        "rjhd,rkhd->rhjk", query_heads, key_heads, preferred_element_type=jnp.float32
    )
    scores = products * score_scale + bias.astype(jnp.float32)[None]
    scores = jnp.where(allowed[None, None], scores, NEGATIVE)
    row_top = jnp.max(scores, axis=3, keepdims=True)
    log_total = row_top + jnp.log(jnp.sum(jnp.exp(scores - row_top), axis=3, keepdims=True))
    weights = jnp.exp(scores - log_total)
    probs = weights.astype(jnp.bfloat16)
    attended = jnp.einsum("rhjk,rkhd->rjhd", probs, value_heads, preferred_element_type=jnp.float32)

    gate_sig = jax.nn.sigmoid(gate.astype(jnp.float32)).reshape(
        slab_rows, local_cols, head_count, head_size
    )
    cotangent = grad_out.astype(jnp.float32).reshape(slab_rows, local_cols, head_count, head_size)
    gate_grad = (
        (cotangent * attended * gate_sig * (1.0 - gate_sig))
        .astype(jnp.bfloat16)
        .reshape(slab_rows, local_cols, channels)
    )
    out_grad = (cotangent * gate_sig).astype(jnp.bfloat16)
    grad_dot = jnp.transpose(jnp.sum(out_grad.astype(jnp.float32) * attended, axis=3), (0, 2, 1))

    prob_grad = jnp.einsum(
        "rjhd,rkhd->rhjk", out_grad, value_heads, preferred_element_type=jnp.float32
    )
    score_grad = weights * (prob_grad - grad_dot[..., None])
    score_grad_b = score_grad.astype(jnp.bfloat16)
    query_acc = jnp.einsum(
        "rhjk,rkhd->rjhd", score_grad_b, key_heads, preferred_element_type=jnp.float32
    )
    key_part = jnp.einsum(
        "rhjk,rjhd->rkhd", score_grad_b, query_heads, preferred_element_type=jnp.float32
    ).reshape(slab_rows, all_cols, channels)
    value_part = jnp.einsum(
        "rhjk,rjhd->rkhd", probs, out_grad, preferred_element_type=jnp.float32
    ).reshape(slab_rows, all_cols, channels)
    kv_part = jnp.concatenate((key_part, value_part), axis=2).astype(jnp.bfloat16)
    bias_part = jnp.sum(score_grad, axis=0).astype(jnp.bfloat16)

    col_count = all_cols // local_cols
    kv_moved = lax.all_to_all(
        kv_part.reshape(slab_rows, col_count, local_cols, 2 * channels), "col", 1, 1, tiled=True
    )
    kv_sum = jnp.sum(kv_moved.astype(jnp.float32), axis=1)
    key_grad = (kv_sum[..., :channels] * score_scale).astype(jnp.bfloat16)
    value_grad = kv_sum[..., channels:].astype(jnp.bfloat16)
    row_count = lax.axis_size("row")
    row_keys = all_cols // row_count
    bias_moved = lax.all_to_all(
        bias_part.reshape(head_count, local_cols, row_count, row_keys), "row", 2, 2, tiled=True
    )
    bias_grad = jnp.sum(bias_moved.astype(jnp.float32), axis=2)
    query_grad = (
        (query_acc * score_scale).astype(jnp.bfloat16).reshape(slab_rows, local_cols, channels)
    )
    return (query_grad, key_grad, value_grad, gate_grad, bias_grad)


def solution(mesh):
    return jax.shard_map(
        local,
        mesh=mesh,
        in_specs=(
            P("row", "col", None),
            P("row", "col", None),
            P("row", "col", None),
            P("row", "col", None),
            P(None, "col", None),
            P("row", "col", None),
            P(),
        ),
        out_specs=(
            P("row", "col", None),
            P("row", "col", None),
            P("row", "col", None),
            P("row", "col", None),
            P(None, "col", "row"),
        ),
        check_vma=False,
    )
```

```python
import math

import jax
import jax.numpy as jnp
from jax import lax
from jax.sharding import PartitionSpec as P

H = 4
DH = 32
BLK = 128


NEGATIVE = -1000000000.0


def local(queries, keys, values, gate, bias, grad_out, block_mask):
    slab_rows, local_cols, channels = queries.shape
    head_count = H
    head_size = DH
    score_scale = 1.0 / math.sqrt(head_size)
    col_start = lax.axis_index("col") * local_cols
    kv_all = lax.all_gather(jnp.concatenate((keys, values), axis=2), "col", axis=1, tiled=True)
    key_all = kv_all[..., :channels]
    value_all = kv_all[..., channels:]
    all_cols = key_all.shape[1]
    query_heads = queries.reshape(slab_rows, local_cols, head_count, head_size)
    key_heads = key_all.reshape(slab_rows, all_cols, head_count, head_size)
    value_heads = value_all.reshape(slab_rows, all_cols, head_count, head_size)

    block_ids = (col_start + jnp.arange(local_cols, dtype=jnp.int32)) // BLK
    allowed = jnp.repeat(jnp.take(block_mask, block_ids, axis=0), BLK, axis=1) > 0

    products = jnp.einsum(
        "rjhd,rkhd->rhjk", query_heads, key_heads, preferred_element_type=jnp.float32
    )
    scores = products * score_scale + bias.astype(jnp.float32)[None]
    scores = jnp.where(allowed[None, None], scores, NEGATIVE)
    row_top = jnp.max(scores, axis=3, keepdims=True)
    log_total = row_top + jnp.log(jnp.sum(jnp.exp(scores - row_top), axis=3, keepdims=True))
    weights = jnp.exp(scores - log_total)
    probs = weights.astype(jnp.bfloat16)
    attended = jnp.einsum("rhjk,rkhd->rjhd", probs, value_heads, preferred_element_type=jnp.float32)

    gate_sig = jax.nn.sigmoid(gate.astype(jnp.float32)).reshape(
        slab_rows, local_cols, head_count, head_size
    )
    cotangent = grad_out.astype(jnp.float32).reshape(slab_rows, local_cols, head_count, head_size)
    gate_grad = (
        (cotangent * attended * gate_sig * (1.0 - gate_sig))
        .astype(jnp.bfloat16)
        .reshape(slab_rows, local_cols, channels)
    )
    out_grad = (cotangent * gate_sig).astype(jnp.bfloat16)
    grad_dot = jnp.transpose(jnp.sum(out_grad.astype(jnp.float32) * attended, axis=3), (0, 2, 1))

    prob_grad = jnp.einsum(
        "rjhd,rkhd->rhjk", out_grad, value_heads, preferred_element_type=jnp.float32
    )
    score_grad = weights * (prob_grad - grad_dot[..., None])
    score_grad_b = score_grad.astype(jnp.bfloat16)
    query_acc = jnp.einsum(
        "rhjk,rkhd->rjhd", score_grad_b, key_heads, preferred_element_type=jnp.float32
    )
    key_part = jnp.einsum(
        "rhjk,rjhd->rkhd", score_grad_b, query_heads, preferred_element_type=jnp.float32
    ).reshape(slab_rows, all_cols, channels)
    value_part = jnp.einsum(
        "rhjk,rjhd->rkhd", probs, out_grad, preferred_element_type=jnp.float32
    ).reshape(slab_rows, all_cols, channels)
    kv_part = jnp.concatenate((key_part, value_part), axis=2).astype(jnp.bfloat16)
    bias_part = jnp.sum(score_grad, axis=0).astype(jnp.bfloat16)

    col_count = all_cols // local_cols
    kv_moved = lax.all_to_all(
        kv_part.reshape(slab_rows, col_count, local_cols, 2 * channels), "col", 1, 1, tiled=True
    )
    kv_sum = jnp.sum(kv_moved.astype(jnp.float32), axis=1)
    key_grad = (kv_sum[..., :channels] * score_scale).astype(jnp.bfloat16)
    value_grad = kv_sum[..., channels:].astype(jnp.bfloat16)
    row_count = lax.axis_size("row")
    row_keys = all_cols // row_count
    bias_moved = lax.all_to_all(
        bias_part.reshape(head_count, local_cols, row_count, row_keys), "row", 2, 2, tiled=True
    )
    bias_grad = jnp.sum(bias_moved.astype(jnp.float32), axis=2)
    query_grad = (
        (query_acc * score_scale).astype(jnp.bfloat16).reshape(slab_rows, local_cols, channels)
    )
    return (query_grad, key_grad, value_grad, gate_grad, bias_grad)


def solution(mesh):
    return jax.shard_map(
        local,
        mesh=mesh,
        in_specs=(
            P("row", "col", None),
            P("row", "col", None),
            P("row", "col", None),
            P("row", "col", None),
            P(None, "col", None),
            P("row", "col", None),
            P(),
        ),
        out_specs=(
            P("row", "col", None),
            P("row", "col", None),
            P("row", "col", None),
            P("row", "col", None),
            P(None, "col", "row"),
        ),
        check_vma=False,
    )
```

```python
import math

import jax
import jax.numpy as jnp
from jax import lax
from jax.sharding import PartitionSpec as P

H = 4
DH = 32
BLK = 128


NEGATIVE = -1000000000.0


def local(queries, keys, values, gate, bias, grad_out, block_mask):
    slab_rows, local_cols, channels = queries.shape
    head_count = H
    head_size = DH
    score_scale = 1.0 / math.sqrt(head_size)
    col_start = lax.axis_index("col") * local_cols
    col_count = lax.axis_size("col")
    kv_local = jnp.concatenate((keys, values), axis=2)
    kv_copies = jnp.broadcast_to(kv_local[:, None], (slab_rows, col_count) + kv_local.shape[1:])
    kv_all = lax.all_to_all(kv_copies, "col", 1, 1, tiled=True).reshape(
        slab_rows, col_count * local_cols, 2 * channels
    )
    key_all = kv_all[..., :channels]
    value_all = kv_all[..., channels:]
    all_cols = key_all.shape[1]
    query_heads = queries.reshape(slab_rows, local_cols, head_count, head_size)
    key_heads = key_all.reshape(slab_rows, all_cols, head_count, head_size)
    value_heads = value_all.reshape(slab_rows, all_cols, head_count, head_size)

    block_ids = (col_start + jnp.arange(local_cols, dtype=jnp.int32)) // BLK
    allowed = jnp.repeat(jnp.take(block_mask, block_ids, axis=0), BLK, axis=1) > 0

    products = jnp.einsum(
        "rjhd,rkhd->rhjk", query_heads, key_heads, preferred_element_type=jnp.float32
    )
    scores = products * score_scale + bias.astype(jnp.float32)[None]
    scores = jnp.where(allowed[None, None], scores, NEGATIVE)
    row_top = jnp.max(scores, axis=3, keepdims=True)
    log_total = row_top + jnp.log(jnp.sum(jnp.exp(scores - row_top), axis=3, keepdims=True))
    weights = jnp.exp(scores - log_total)
    probs = weights.astype(jnp.bfloat16)
    attended = jnp.einsum("rhjk,rkhd->rjhd", probs, value_heads, preferred_element_type=jnp.float32)

    gate_sig = jax.nn.sigmoid(gate.astype(jnp.float32)).reshape(
        slab_rows, local_cols, head_count, head_size
    )
    cotangent = grad_out.astype(jnp.float32).reshape(slab_rows, local_cols, head_count, head_size)
    gate_grad = (
        (cotangent * attended * gate_sig * (1.0 - gate_sig))
        .astype(jnp.bfloat16)
        .reshape(slab_rows, local_cols, channels)
    )
    out_grad = (cotangent * gate_sig).astype(jnp.bfloat16)
    grad_dot = jnp.transpose(jnp.sum(out_grad.astype(jnp.float32) * attended, axis=3), (0, 2, 1))

    prob_grad = jnp.einsum(
        "rjhd,rkhd->rhjk", out_grad, value_heads, preferred_element_type=jnp.float32
    )
    score_grad = weights * (prob_grad - grad_dot[..., None])
    score_grad_b = score_grad.astype(jnp.bfloat16)
    query_acc = jnp.einsum(
        "rhjk,rkhd->rjhd", score_grad_b, key_heads, preferred_element_type=jnp.float32
    )
    key_part = jnp.einsum(
        "rhjk,rjhd->rkhd", score_grad_b, query_heads, preferred_element_type=jnp.float32
    ).reshape(slab_rows, all_cols, channels)
    value_part = jnp.einsum(
        "rhjk,rjhd->rkhd", probs, out_grad, preferred_element_type=jnp.float32
    ).reshape(slab_rows, all_cols, channels)
    kv_part = jnp.concatenate((key_part, value_part), axis=2).astype(jnp.bfloat16)
    bias_part = jnp.sum(score_grad, axis=0).astype(jnp.bfloat16)

    kv_moved = lax.all_to_all(
        kv_part.reshape(slab_rows, col_count, local_cols, 2 * channels), "col", 1, 1, tiled=True
    )
    kv_sum = jnp.sum(kv_moved.astype(jnp.float32), axis=1)
    key_grad = (kv_sum[..., :channels] * score_scale).astype(jnp.bfloat16)
    value_grad = kv_sum[..., channels:].astype(jnp.bfloat16)
    row_count = lax.axis_size("row")
    row_keys = all_cols // row_count
    row_index = lax.axis_index("row")
    bias_chunks = bias_part.reshape(head_count, local_cols, row_count, row_keys)
    bias_grad = lax.dynamic_index_in_dim(bias_chunks, row_index, 2, keepdims=False).astype(
        jnp.float32
    )
    for shift in range(1, row_count):
        chunk = lax.dynamic_index_in_dim(
            bias_chunks, (row_index + shift) % row_count, 2, keepdims=False
        )
        moved = lax.ppermute(
            chunk, "row", [(src, (src + shift) % row_count) for src in range(row_count)]
        )
        bias_grad = bias_grad + moved.astype(jnp.float32)
    query_grad = (
        (query_acc * score_scale).astype(jnp.bfloat16).reshape(slab_rows, local_cols, channels)
    )
    return (query_grad, key_grad, value_grad, gate_grad, bias_grad)


def solution(mesh):
    return jax.shard_map(
        local,
        mesh=mesh,
        in_specs=(
            P("row", "col", None),
            P("row", "col", None),
            P("row", "col", None),
            P("row", "col", None),
            P(None, "col", None),
            P("row", "col", None),
            P(),
        ),
        out_specs=(
            P("row", "col", None),
            P("row", "col", None),
            P("row", "col", None),
            P("row", "col", None),
            P(None, "col", "row"),
        ),
        check_vma=False,
    )
```

```python
import math

import jax
import jax.numpy as jnp
from jax import lax
from jax.sharding import PartitionSpec as P

H = 4
DH = 32
BLK = 128


NEGATIVE = -1000000000.0


def slab_grads(queries, keys, values, gate, bias, grad_out, allowed):
    slab_rows, local_cols, channels = queries.shape
    head_count = H
    head_size = DH
    score_scale = 1.0 / math.sqrt(head_size)
    col_count = lax.axis_size("col")
    kv_local = jnp.concatenate((keys, values), axis=2)
    kv_copies = jnp.broadcast_to(kv_local[:, None], (slab_rows, col_count) + kv_local.shape[1:])
    kv_all = lax.all_to_all(kv_copies, "col", 1, 1, tiled=True).reshape(
        slab_rows, col_count * local_cols, 2 * channels
    )
    key_all = kv_all[..., :channels]
    value_all = kv_all[..., channels:]
    all_cols = key_all.shape[1]
    query_heads = queries.reshape(slab_rows, local_cols, head_count, head_size)
    key_heads = key_all.reshape(slab_rows, all_cols, head_count, head_size)
    value_heads = value_all.reshape(slab_rows, all_cols, head_count, head_size)

    products = jnp.einsum(
        "rjhd,rkhd->rhjk", query_heads, key_heads, preferred_element_type=jnp.float32
    )
    scores = products * score_scale + bias.astype(jnp.float32)[None]
    scores = jnp.where(allowed[None, None], scores, NEGATIVE)
    row_top = jnp.max(scores, axis=3, keepdims=True)
    log_total = row_top + jnp.log(jnp.sum(jnp.exp(scores - row_top), axis=3, keepdims=True))
    weights = jnp.exp(scores - log_total)
    probs = weights.astype(jnp.bfloat16)
    attended = jnp.einsum("rhjk,rkhd->rjhd", probs, value_heads, preferred_element_type=jnp.float32)

    gate_sig = jax.nn.sigmoid(gate.astype(jnp.float32)).reshape(
        slab_rows, local_cols, head_count, head_size
    )
    cotangent = grad_out.astype(jnp.float32).reshape(slab_rows, local_cols, head_count, head_size)
    gate_grad = (
        (cotangent * attended * gate_sig * (1.0 - gate_sig))
        .astype(jnp.bfloat16)
        .reshape(slab_rows, local_cols, channels)
    )
    out_grad = (cotangent * gate_sig).astype(jnp.bfloat16)
    grad_dot = jnp.transpose(jnp.sum(out_grad.astype(jnp.float32) * attended, axis=3), (0, 2, 1))

    prob_grad = jnp.einsum(
        "rjhd,rkhd->rhjk", out_grad, value_heads, preferred_element_type=jnp.float32
    )
    score_grad = weights * (prob_grad - grad_dot[..., None])
    score_grad_b = score_grad.astype(jnp.bfloat16)
    query_acc = jnp.einsum(
        "rhjk,rkhd->rjhd", score_grad_b, key_heads, preferred_element_type=jnp.float32
    )
    key_part = jnp.einsum(
        "rhjk,rjhd->rkhd", score_grad_b, query_heads, preferred_element_type=jnp.float32
    ).reshape(slab_rows, all_cols, channels)
    value_part = jnp.einsum(
        "rhjk,rjhd->rkhd", probs, out_grad, preferred_element_type=jnp.float32
    ).reshape(slab_rows, all_cols, channels)
    kv_part = jnp.concatenate((key_part, value_part), axis=2).astype(jnp.bfloat16)
    bias_part = jnp.sum(score_grad, axis=0)

    kv_moved = lax.all_to_all(
        kv_part.reshape(slab_rows, col_count, local_cols, 2 * channels), "col", 1, 1, tiled=True
    )
    kv_sum = jnp.sum(kv_moved.astype(jnp.float32), axis=1)
    key_grad = (kv_sum[..., :channels] * score_scale).astype(jnp.bfloat16)
    value_grad = kv_sum[..., channels:].astype(jnp.bfloat16)
    query_grad = (
        (query_acc * score_scale).astype(jnp.bfloat16).reshape(slab_rows, local_cols, channels)
    )
    return (query_grad, key_grad, value_grad, gate_grad, bias_part)


def local(queries, keys, values, gate, bias, grad_out, block_mask):
    slab_rows, local_cols, channels = queries.shape
    all_cols = bias.shape[2]
    col_start = lax.axis_index("col") * local_cols
    block_ids = (col_start + jnp.arange(local_cols, dtype=jnp.int32)) // BLK
    allowed = jnp.repeat(jnp.take(block_mask, block_ids, axis=0), BLK, axis=1) > 0

    pieces = [
        slab_grads(
            queries[row : row + 1],
            keys[row : row + 1],
            values[row : row + 1],
            gate[row : row + 1],
            bias,
            grad_out[row : row + 1],
            allowed,
        )
        for row in range(slab_rows)
    ]
    query_grad, key_grad, value_grad, gate_grad = (
        jnp.concatenate([piece[n] for piece in pieces], axis=0) for n in range(4)
    )
    bias_sum = pieces[0][4]
    for piece in pieces[1:]:
        bias_sum = bias_sum + piece[4]
    bias_part = bias_sum.astype(jnp.bfloat16)

    row_count = lax.axis_size("row")
    row_keys = all_cols // row_count
    row_index = lax.axis_index("row")
    bias_chunks = bias_part.reshape(H, local_cols, row_count, row_keys)
    bias_grad = lax.dynamic_index_in_dim(bias_chunks, row_index, 2, keepdims=False).astype(
        jnp.float32
    )
    for shift in range(1, row_count):
        chunk = lax.dynamic_index_in_dim(
            bias_chunks, (row_index + shift) % row_count, 2, keepdims=False
        )
        moved = lax.ppermute(
            chunk, "row", [(src, (src + shift) % row_count) for src in range(row_count)]
        )
        bias_grad = bias_grad + moved.astype(jnp.float32)
    return (query_grad, key_grad, value_grad, gate_grad, bias_grad)


def solution(mesh):
    return jax.shard_map(
        local,
        mesh=mesh,
        in_specs=(
            P("row", "col", None),
            P("row", "col", None),
            P("row", "col", None),
            P("row", "col", None),
            P(None, "col", None),
            P("row", "col", None),
            P(),
        ),
        out_specs=(
            P("row", "col", None),
            P("row", "col", None),
            P("row", "col", None),
            P("row", "col", None),
            P(None, "col", "row"),
        ),
        check_vma=False,
    )
```

```python
import math

import jax
import jax.numpy as jnp
from jax import lax
from jax.sharding import PartitionSpec as P

H = 4
DH = 32
BLK = 128


NEGATIVE = -1000000000.0


def local(queries, keys, values, gate, bias, grad_out, block_mask):
    slab_rows, local_cols, channels = queries.shape
    head_count = H
    head_size = DH
    score_scale = 1.0 / math.sqrt(head_size)
    col_start = lax.axis_index("col") * local_cols
    col_count = lax.axis_size("col")
    kv_local = jnp.concatenate((keys, values), axis=2)
    kv_copies = jnp.broadcast_to(kv_local[:, None], (slab_rows, col_count) + kv_local.shape[1:])
    kv_all = lax.all_to_all(kv_copies, "col", 1, 1, tiled=True).reshape(
        slab_rows, col_count * local_cols, 2 * channels
    )
    key_all = kv_all[..., :channels]
    value_all = kv_all[..., channels:]
    all_cols = key_all.shape[1]
    query_heads = queries.reshape(slab_rows, local_cols, head_count, head_size)
    key_heads = key_all.reshape(slab_rows, all_cols, head_count, head_size)
    value_heads = value_all.reshape(slab_rows, all_cols, head_count, head_size)

    block_ids = (col_start + jnp.arange(local_cols, dtype=jnp.int32)) // BLK
    allowed = jnp.repeat(jnp.take(block_mask, block_ids, axis=0), BLK, axis=1) > 0

    products = jnp.einsum(
        "rjhd,rkhd->rhjk", query_heads, key_heads, preferred_element_type=jnp.float32
    )
    scores = products * score_scale + bias.astype(jnp.float32)[None]
    scores = jnp.where(allowed[None, None], scores, NEGATIVE)
    row_top = jnp.max(scores, axis=3, keepdims=True)
    log_total = row_top + jnp.log(jnp.sum(jnp.exp(scores - row_top), axis=3, keepdims=True))
    weights = jnp.exp(scores - log_total)
    probs = weights.astype(jnp.bfloat16)
    attended = jnp.einsum("rhjk,rkhd->rjhd", probs, value_heads, preferred_element_type=jnp.float32)

    gate_sig = jax.nn.sigmoid(gate.astype(jnp.float32)).reshape(
        slab_rows, local_cols, head_count, head_size
    )
    cotangent = grad_out.astype(jnp.float32).reshape(slab_rows, local_cols, head_count, head_size)
    gate_grad = (
        (cotangent * attended * gate_sig * (1.0 - gate_sig))
        .astype(jnp.bfloat16)
        .reshape(slab_rows, local_cols, channels)
    )
    out_grad = (cotangent * gate_sig).astype(jnp.bfloat16)
    grad_dot = jnp.transpose(jnp.sum(out_grad.astype(jnp.float32) * attended, axis=3), (0, 2, 1))

    prob_grad = jnp.einsum(
        "rjhd,rkhd->rhjk", out_grad, value_heads, preferred_element_type=jnp.float32
    )
    score_grad = weights * (prob_grad - grad_dot[..., None])
    score_grad_b = score_grad.astype(jnp.bfloat16)
    query_acc = jnp.einsum(
        "rhjk,rkhd->rjhd", score_grad_b, key_heads, preferred_element_type=jnp.float32
    )
    key_part = jnp.einsum(
        "rhjk,rjhd->rkhd", score_grad_b, query_heads, preferred_element_type=jnp.float32
    ).reshape(slab_rows, all_cols, channels)
    value_part = jnp.einsum(
        "rhjk,rjhd->rkhd", probs, out_grad, preferred_element_type=jnp.float32
    ).reshape(slab_rows, all_cols, channels)
    kv_part = jnp.concatenate((key_part, value_part), axis=2).astype(jnp.bfloat16)
    bias_part = jnp.sum(score_grad, axis=0).astype(jnp.bfloat16)

    kv_moved = lax.all_to_all(
        kv_part.reshape(slab_rows, col_count, local_cols, 2 * channels), "col", 1, 1, tiled=True
    )
    kv_sum = jnp.sum(kv_moved.astype(jnp.float32), axis=1)
    key_grad = (kv_sum[..., :channels] * score_scale).astype(jnp.bfloat16)
    value_grad = kv_sum[..., channels:].astype(jnp.bfloat16)
    row_count = lax.axis_size("row")
    row_keys = all_cols // row_count
    row_index = lax.axis_index("row")
    bias_blocks = bias_part.reshape(head_count, local_cols, row_count, row_keys)
    kv_moved, head_blocks = lax.optimization_barrier((kv_moved, bias_blocks[:1]))
    head_moved = lax.all_to_all(head_blocks, "row", 2, 2, tiled=True)
    head_grad = jnp.sum(head_moved.astype(jnp.float32), axis=2)
    bias_chunks = bias_blocks[1:]
    bias_grad = lax.dynamic_index_in_dim(bias_chunks, row_index, 2, keepdims=False).astype(
        jnp.float32
    )
    for shift in range(1, row_count):
        chunk = lax.dynamic_index_in_dim(
            bias_chunks, (row_index + shift) % row_count, 2, keepdims=False
        )
        moved = lax.ppermute(
            chunk, "row", [(src, (src + shift) % row_count) for src in range(row_count)]
        )
        bias_grad = bias_grad + moved.astype(jnp.float32)
    bias_grad = jnp.concatenate((head_grad, bias_grad), axis=0)
    query_grad = (
        (query_acc * score_scale).astype(jnp.bfloat16).reshape(slab_rows, local_cols, channels)
    )
    return (query_grad, key_grad, value_grad, gate_grad, bias_grad)


def solution(mesh):
    return jax.shard_map(
        local,
        mesh=mesh,
        in_specs=(
            P("row", "col", None),
            P("row", "col", None),
            P("row", "col", None),
            P("row", "col", None),
            P(None, "col", None),
            P("row", "col", None),
            P(),
        ),
        out_specs=(
            P("row", "col", None),
            P("row", "col", None),
            P("row", "col", None),
            P("row", "col", None),
            P(None, "col", "row"),
        ),
        check_vma=False,
    )
```

```python
import math

import jax
import jax.numpy as jnp
from jax import lax
from jax.sharding import PartitionSpec as P

H = 4
DH = 32
BLK = 128


NEGATIVE = -1000000000.0


def local(queries, keys, values, gate, bias, grad_out, block_mask):
    slab_rows, local_cols, channels = queries.shape
    head_count = H
    head_size = DH
    score_scale = 1.0 / math.sqrt(head_size)
    col_start = lax.axis_index("col") * local_cols
    col_count = lax.axis_size("col")
    kv_local = jnp.concatenate((keys, values), axis=2)
    kv_copies = jnp.broadcast_to(kv_local[:, None], (slab_rows, col_count) + kv_local.shape[1:])
    kv_all = lax.all_to_all(kv_copies, "col", 1, 1, tiled=True).reshape(
        slab_rows, col_count * local_cols, 2 * channels
    )
    key_all = kv_all[..., :channels]
    value_all = kv_all[..., channels:]
    all_cols = key_all.shape[1]
    query_heads = queries.reshape(slab_rows, local_cols, head_count, head_size)
    key_heads = key_all.reshape(slab_rows, all_cols, head_count, head_size)
    value_heads = value_all.reshape(slab_rows, all_cols, head_count, head_size)

    block_ids = (col_start + jnp.arange(local_cols, dtype=jnp.int32)) // BLK
    allowed = jnp.repeat(jnp.take(block_mask, block_ids, axis=0), BLK, axis=1) > 0

    products = jnp.einsum(
        "rjhd,rkhd->rhjk", query_heads, key_heads, preferred_element_type=jnp.float32
    )
    scores = products * score_scale + bias.astype(jnp.float32)[None]
    scores = jnp.where(allowed[None, None], scores, NEGATIVE)
    row_top = jnp.max(scores, axis=3, keepdims=True)
    log_total = row_top + jnp.log(jnp.sum(jnp.exp(scores - row_top), axis=3, keepdims=True))
    weights = jnp.exp(scores - log_total)
    probs = weights.astype(jnp.bfloat16)
    attended = jnp.einsum("rhjk,rkhd->rjhd", probs, value_heads, preferred_element_type=jnp.float32)

    gate_sig = jax.nn.sigmoid(gate.astype(jnp.float32)).reshape(
        slab_rows, local_cols, head_count, head_size
    )
    cotangent = grad_out.astype(jnp.float32).reshape(slab_rows, local_cols, head_count, head_size)
    gate_grad = (
        (cotangent * attended * gate_sig * (1.0 - gate_sig))
        .astype(jnp.bfloat16)
        .reshape(slab_rows, local_cols, channels)
    )
    out_grad = (cotangent * gate_sig).astype(jnp.bfloat16)
    grad_dot = jnp.transpose(jnp.sum(out_grad.astype(jnp.float32) * attended, axis=3), (0, 2, 1))

    prob_grad = jnp.einsum(
        "rjhd,rkhd->rhjk", out_grad, value_heads, preferred_element_type=jnp.float32
    )
    score_grad = weights * (prob_grad - grad_dot[..., None])
    score_grad_b = score_grad.astype(jnp.bfloat16)
    query_acc = jnp.einsum(
        "rhjk,rkhd->rjhd", score_grad_b, key_heads, preferred_element_type=jnp.float32
    )
    key_part = jnp.einsum(
        "rhjk,rjhd->rkhd", score_grad_b, query_heads, preferred_element_type=jnp.float32
    ).reshape(slab_rows, all_cols, channels)
    value_part = jnp.einsum(
        "rhjk,rjhd->rkhd", probs, out_grad, preferred_element_type=jnp.float32
    ).reshape(slab_rows, all_cols, channels)
    kv_part = jnp.concatenate((key_part, value_part), axis=2).astype(jnp.bfloat16)
    bias_part = jnp.sum(score_grad, axis=0).astype(jnp.bfloat16)

    row_count = lax.axis_size("row")
    row_keys = all_cols // row_count
    bias_moved = lax.all_to_all(
        bias_part.reshape(head_count, local_cols, row_count, row_keys), "row", 2, 2, tiled=True
    )
    bias_grad = jnp.sum(bias_moved.astype(jnp.float32), axis=2)
    col_index = lax.axis_index("col")
    kv_chunks = kv_part.reshape(slab_rows, col_count, local_cols, 2 * channels)
    kv_sum = lax.dynamic_index_in_dim(kv_chunks, col_index, 1, keepdims=False).astype(jnp.float32)
    for shift in range(1, col_count):
        chunk = lax.dynamic_index_in_dim(kv_chunks, (col_index + shift) % col_count, 1, keepdims=False)
        moved = lax.ppermute(
            chunk, "col", [(src, (src + shift) % col_count) for src in range(col_count)]
        )
        kv_sum = kv_sum + moved.astype(jnp.float32)
    key_grad = (kv_sum[..., :channels] * score_scale).astype(jnp.bfloat16)
    value_grad = kv_sum[..., channels:].astype(jnp.bfloat16)
    query_grad = (
        (query_acc * score_scale).astype(jnp.bfloat16).reshape(slab_rows, local_cols, channels)
    )
    return (query_grad, key_grad, value_grad, gate_grad, bias_grad)


def solution(mesh):
    return jax.shard_map(
        local,
        mesh=mesh,
        in_specs=(
            P("row", "col", None),
            P("row", "col", None),
            P("row", "col", None),
            P("row", "col", None),
            P(None, "col", None),
            P("row", "col", None),
            P(),
        ),
        out_specs=(
            P("row", "col", None),
            P("row", "col", None),
            P("row", "col", None),
            P("row", "col", None),
            P(None, "col", "row"),
        ),
        check_vma=False,
    )
```
